256 devices in a mesh: comp: 32 (over y, x, core), prompt: 8 (over z).
Axes of the slice: x: 4, y: 4, z: 8, core: 2. Of those that a mesh axis runs over, the one named last changes fastest.
Arguments:
- queries: bfloat16 [65536, 2560], P(('prompt', 'comp')), parts along dimension 0, may hold values from -128 to 128, as said below
- suffix_key_value: bfloat16 [2, 65536, 512], P(None, ('prompt', 'comp')), parts along dimension 1, may hold values from -6 to 6
- output_gradient: bfloat16 [65536, 2560], P(('prompt', 'comp')), parts along dimension 0, may hold values from -96 to 96
- node_kv: bfloat16 [256, 2, 128, 512], P(('prompt', 'comp')), parts along dimension 0, may hold values from -8 to 8, as said below
- paths: int32 [512, 4], P(('prompt', 'comp')), parts along dimension 0, may hold values from 0 to 31, as said below
- tile_lens: int32 [256], P('prompt'), parts along dimension 0, may hold values from 1 to 128, as said below
Outputs:
- query_out: bfloat16 [65536, 2560], P(('prompt', 'comp')), parts along dimension 0
- suffix_out: bfloat16 [2, 65536, 512], P(None, ('prompt', 'comp')), parts along dimension 1
- node_out: bfloat16 [256, 2, 128, 512], P(('prompt', 'comp')), parts along dimension 0
The draws below stay inside these ranges and needn't reach their ends.
There are 8 independent parts, one for each index of `prompt`. The reference program is written for one: setup_inputs(seed, part) draws one part's arguments, and reference() takes and returns one part's arrays. A program takes and returns all parts, laid end to end along the dimension named above; each array names one. Nothing has to cross between parts.
Inputs may be any that keep to these rules, and one draw needn't show every extreme that they name: paths[c] are the 4 trie nodes of completion c from the root down; every completion has the same root, the completions of one block of 2 share their second node, and each node has one parent; node n's tile is row n of node_kv, values are node numbers below 32. `tile_lens`: the root's tile is full. real-valued queries. `node_kv`: real-valued keys and values.
All inputs are finite; a program needn't handle non-finite values.
Results may differ from the reference program's by a relative error of at most 0.02.
Values may be sent and summed in bfloat16 or wider, within the bound.
No kernel may reach another device: no remote copies, remote signals or barrier semaphores. Data moves between devices by JAX's collectives and lax.ppermute only.
A program may use at most 128 MiB of HBM per device.

```python
import math
import jax
import jax.numpy as jnp
from jax import lax

QUERY_HEADS = 20
KV_HEADS = 4
HEAD_SIZE = 128
TILE_SLOTS = 128
DEPTH = 4
QUERY_LENGTH = 128
COMP_DEV = 2
SAMPLE_COUNT = 64
TRIE_NODES = 32
N_COMP = 32


def trie_layout(key):
    seeded = jax.random.fold_in(key, 7)
    labels = jax.random.permutation(jax.random.fold_in(seeded, 1), TRIE_NODES).astype(jnp.int32)
    level_one = TRIE_NODES // 8
    level_two = TRIE_NODES // 4
    owners = jnp.arange(SAMPLE_COUNT, dtype=jnp.int32) // COMP_DEV
    branch = jax.random.randint(jax.random.fold_in(seeded, 2), (SAMPLE_COUNT // COMP_DEV,), 0, level_one)[owners]
    within = jax.random.randint(jax.random.fold_in(seeded, 3), (SAMPLE_COUNT,), 0, 4)
    within = within.at[1].set(jnp.bitwise_xor(within[0], 2))
    leaf_index = branch * 4 + within
    positions = jnp.stack([jnp.zeros_like(leaf_index), 1 + branch, 1 + level_one + leaf_index // 2, 1 + level_one + level_two + leaf_index], axis=1)
    return (labels, labels[positions].astype(jnp.int32))


def node_values(key):
    tile_value_rows = jnp.clip(jax.random.normal(jax.random.fold_in(key, 21), (TRIE_NODES, 2, TILE_SLOTS, KV_HEADS * HEAD_SIZE), jnp.float32), -6.0, 6.0)
    labels, drawn_paths = trie_layout(key)
    root_node = labels[0]
    nearby = 0.99 * tile_value_rows[root_node, 0, 0] + 0.14 * tile_value_rows[root_node, 0, 1]
    return tile_value_rows.at[root_node, 0, 1].set(nearby)


def draw_node_kv(key, part):
    return node_values(key).astype(jnp.bfloat16)


def draw_paths(key, part):
    return trie_layout(key)[1]


def draw_tile_lens(key, part):
    labels = trie_layout(key)[0]
    valid = jax.random.randint(jax.random.fold_in(key, 11), (TRIE_NODES,), 1, TILE_SLOTS + 1)
    return valid.at[labels[0]].set(TILE_SLOTS).at[labels[1]].set(1).astype(jnp.int32)


def draw_queries(key, part):
    rows_total = SAMPLE_COUNT * QUERY_LENGTH
    queries = jax.random.normal(jax.random.fold_in(key, 31), (rows_total, QUERY_HEADS * HEAD_SIZE), jnp.float32)
    return queries.astype(jnp.bfloat16)


def steps_of(key, dims, cuts, smallest, high):
    loudness = 1.0
    for axis_at, parts in cuts:
        draws = jax.random.uniform(jax.random.fold_in(jax.random.fold_in(key, 6), axis_at), (parts,), jnp.float32, smallest / len(cuts), high / len(cuts))
        loudness = loudness * jnp.repeat(jnp.exp(draws), dims[axis_at] // parts).reshape((-1,) + (1,) * (len(dims) - 1 - axis_at))
    return loudness


def bell_draw(rng, shape, width, limit, shards=(), held_as=jnp.bfloat16):
    drawn = width * jax.random.normal(rng, shape, jnp.float32)
    if shards:
        drawn = drawn * steps_of(rng, shape, shards, -0.22, 0.18)
    return jnp.clip(drawn, -limit, limit).astype(held_as)


def setup_inputs(seed: int = 0, part: int = 0) -> dict:
    arg_keys = jax.random.split(jax.random.key(seed), 7)
    part_keys = jax.random.split(jax.random.fold_in(arg_keys[6], part), 7)
    queries = draw_queries(jax.random.fold_in(jax.random.fold_in(arg_keys[6], part), 71), part)
    suffix_key_value = bell_draw(part_keys[1], (2, SAMPLE_COUNT * QUERY_LENGTH, KV_HEADS * HEAD_SIZE), 1.0, 6.0, ((1, 32),))
    output_gradient = bell_draw(part_keys[2], (SAMPLE_COUNT * QUERY_LENGTH, QUERY_HEADS * HEAD_SIZE), 16.0, 96.0, ((0, 32),))
    node_kv = draw_node_kv(jax.random.fold_in(jax.random.fold_in(arg_keys[6], part), 71), part)
    paths = draw_paths(jax.random.fold_in(jax.random.fold_in(arg_keys[6], part), 71), part)
    tile_lens = draw_tile_lens(jax.random.fold_in(jax.random.fold_in(arg_keys[6], part), 71), part)
    return dict(queries=queries, suffix_key_value=suffix_key_value, output_gradient=output_gradient, node_kv=node_kv, paths=paths, tile_lens=tile_lens)


def reference(queries, suffix_key_value, output_gradient, node_kv, paths, tile_lens):
    group_share = QUERY_HEADS // KV_HEADS
    factor = 1.0 / math.sqrt(HEAD_SIZE)
    trie_node_rows = DEPTH * TILE_SLOTS
    span_width = KV_HEADS * HEAD_SIZE
    key_gradient_total = trie_node_rows + QUERY_LENGTH
    path_tiles = node_kv[paths]
    valid_len = tile_lens[paths]
    slot_index = jnp.arange(TILE_SLOTS, dtype=jnp.int32)
    causal = jnp.arange(QUERY_LENGTH, dtype=jnp.int32)[None, :] <= jnp.arange(QUERY_LENGTH, dtype=jnp.int32)[:, None]

    def completion(member_flag):
        query_matrix = lax.dynamic_slice_in_dim(queries, member_flag * QUERY_LENGTH, QUERY_LENGTH, 0).astype(jnp.float32).reshape(QUERY_LENGTH, KV_HEADS, group_share, HEAD_SIZE)
        cotangent_rows = lax.dynamic_slice_in_dim(output_gradient, member_flag * QUERY_LENGTH, QUERY_LENGTH, 0).astype(jnp.float32).reshape(QUERY_LENGTH, KV_HEADS, group_share, HEAD_SIZE)
        tile_token_block = lax.dynamic_index_in_dim(path_tiles, member_flag, 0, keepdims=False)
        suffix_rows = lax.dynamic_slice_in_dim(suffix_key_value, member_flag * QUERY_LENGTH, QUERY_LENGTH, 1)
        key_matrix = jnp.concatenate([tile_token_block[:, 0].reshape(trie_node_rows, span_width), suffix_rows[0]], 0).astype(jnp.float32).reshape(key_gradient_total, KV_HEADS, HEAD_SIZE)
        value_matrix = jnp.concatenate([tile_token_block[:, 1].reshape(trie_node_rows, span_width), suffix_rows[1]], 0).astype(jnp.float32).reshape(key_gradient_total, KV_HEADS, HEAD_SIZE)
        lengths_here = lax.dynamic_index_in_dim(valid_len, member_flag, 0, keepdims=False)
        node_seen = (slot_index[None, :] < lengths_here[:, None]).reshape(trie_node_rows)
        visible = jnp.concatenate([jnp.broadcast_to(node_seen[None, :], (QUERY_LENGTH, trie_node_rows)), causal], axis=1)
        scores = jnp.einsum('ihgd,jhd->hgij', query_matrix, key_matrix) * factor
        scores = jnp.where(visible[None, None], scores, -jnp.inf)
        top_score = lax.optimization_barrier(jnp.max(scores, axis=-1, keepdims=True))
        weights = jnp.exp(scores - top_score)
        probs = weights / lax.optimization_barrier(jnp.sum(weights, axis=-1, keepdims=True))
        probs_low = lax.optimization_barrier(probs.astype(jnp.bfloat16)).astype(jnp.float32)
        outputs = jnp.einsum('hgij,jhd->ihgd', probs_low, value_matrix)
        centre = lax.optimization_barrier(jnp.sum(cotangent_rows * outputs, axis=-1))
        prob_grads = jnp.einsum('ihgd,jhd->hgij', cotangent_rows, value_matrix)
        score_grads = probs * (prob_grads - jnp.transpose(centre, (1, 2, 0))[..., None])
        score_low = lax.optimization_barrier(score_grads.astype(jnp.bfloat16)).astype(jnp.float32)
        query_gradient = (jnp.einsum('hgij,jhd->ihgd', score_low, key_matrix) * factor).astype(jnp.bfloat16).reshape(QUERY_LENGTH, QUERY_HEADS * HEAD_SIZE)
        key_gradient = (jnp.einsum('hgij,ihgd->jhd', score_low, query_matrix) * factor).reshape(key_gradient_total, span_width)
        value_gradient = jnp.einsum('hgij,ihgd->jhd', probs_low, cotangent_rows).reshape(key_gradient_total, span_width)
        return (query_gradient, key_gradient, value_gradient)
    query_gradient, key_gradient, value_gradient = lax.map(completion, jnp.arange(SAMPLE_COUNT, dtype=jnp.int32))
    query_out = query_gradient.reshape(SAMPLE_COUNT * QUERY_LENGTH, QUERY_HEADS * HEAD_SIZE)
    suffix_out = jnp.stack([key_gradient[:, trie_node_rows:], value_gradient[:, trie_node_rows:]], axis=0).reshape(2, SAMPLE_COUNT * QUERY_LENGTH, span_width).astype(jnp.bfloat16)
    node_terms = jnp.stack([key_gradient[:, :trie_node_rows].reshape(SAMPLE_COUNT, DEPTH, TILE_SLOTS, span_width), value_gradient[:, :trie_node_rows].reshape(SAMPLE_COUNT, DEPTH, TILE_SLOTS, span_width)], axis=2).reshape(SAMPLE_COUNT * DEPTH, 2, TILE_SLOTS, span_width)
    node_ids = paths.reshape(SAMPLE_COUNT * DEPTH).astype(jnp.int32)
    block_size = COMP_DEV * DEPTH

    def add_block(running, member_flag):
        ids_here = lax.dynamic_slice_in_dim(node_ids, member_flag * block_size, block_size, 0)
        terms_here = lax.dynamic_slice_in_dim(node_terms, member_flag * block_size, block_size, 0)
        block_sum = jnp.zeros((TRIE_NODES, 2, TILE_SLOTS, span_width), jnp.float32).at[ids_here].add(terms_here)
        rounded = lax.optimization_barrier(block_sum.astype(jnp.bfloat16)).astype(jnp.float32)
        return (running + rounded, None)
    running, leftover = lax.scan(add_block, jnp.zeros((TRIE_NODES, 2, TILE_SLOTS, span_width), jnp.float32), jnp.arange(N_COMP, dtype=jnp.int32))
    return (query_out, suffix_out, running.astype(jnp.bfloat16))
```

```python
import functools
import math

import jax
import jax.numpy as jnp
from jax import lax
from jax.experimental import pallas as pl
from jax.experimental.pallas import tpu as pltpu
from jax.sharding import Mesh
from jax.sharding import PartitionSpec as P

QUERY_HEADS = 20
KV_HEADS = 4
HEAD_SIZE = 128
TILE_SLOTS = 128
DEPTH = 4
QUERY_LENGTH = 128
GROUP_SHARE = QUERY_HEADS // KV_HEADS
KEY_ROWS = DEPTH * TILE_SLOTS + QUERY_LENGTH


def attention_kernel(lens_ref, q_ref, do_ref, k_ref, v_ref, dq_ref, dk_ref, dv_ref):
    c = pl.program_id(0)
    factor = 1.0 / math.sqrt(HEAD_SIZE)
    key_block = k_ref[...]
    value_block = v_ref[...]
    col = lax.broadcasted_iota(jnp.int32, (QUERY_LENGTH, KEY_ROWS), 1)
    row = lax.broadcasted_iota(jnp.int32, (QUERY_LENGTH, KEY_ROWS), 0)
    level = col // TILE_SLOTS
    slot = col % TILE_SLOTS
    limit = jnp.where(
        level == 0,
        lens_ref[c, 0],
        jnp.where(level == 1, lens_ref[c, 1], jnp.where(level == 2, lens_ref[c, 2], lens_ref[c, 3])),
    )
    visible = ((level < DEPTH) & (slot < limit)) | (
        (level >= DEPTH) & ((col - DEPTH * TILE_SLOTS) <= row)
    )
    dk_acc = jnp.zeros((KEY_ROWS, HEAD_SIZE), jnp.float32)
    dv_acc = jnp.zeros((KEY_ROWS, HEAD_SIZE), jnp.float32)
    nt = (((1,), (1,)), ((), ()))
    tn = (((0,), (0,)), ((), ()))
    for g in range(GROUP_SHARE):
        cols = slice(g * HEAD_SIZE, (g + 1) * HEAD_SIZE)
        query_g = q_ref[:, cols]
        cot_g = do_ref[:, cols]
        scores = lax.dot_general(query_g, key_block, nt, preferred_element_type=jnp.float32) * factor
        scores = jnp.where(visible, scores, -jnp.inf)
        top = jnp.max(scores, axis=-1, keepdims=True)
        weights = jnp.exp(scores - top)
        probs = weights / jnp.sum(weights, axis=-1, keepdims=True)
        probs_low = probs.astype(jnp.bfloat16)
        outputs = jnp.dot(probs_low, value_block, preferred_element_type=jnp.float32)
        centre = jnp.sum(cot_g.astype(jnp.float32) * outputs, axis=-1, keepdims=True)
        prob_grads = lax.dot_general(cot_g, value_block, nt, preferred_element_type=jnp.float32)
        score_low = (probs * (prob_grads - centre)).astype(jnp.bfloat16)
        dq = jnp.dot(score_low, key_block, preferred_element_type=jnp.float32) * factor
        dq_ref[:, cols] = dq.astype(jnp.bfloat16)
        dk_acc = dk_acc + lax.dot_general(score_low, query_g, tn, preferred_element_type=jnp.float32)
        dv_acc = dv_acc + lax.dot_general(probs_low, cot_g, tn, preferred_element_type=jnp.float32)
    dk_ref[...] = dk_acc * factor
    dv_ref[...] = dv_acc


def attention(lens, queries, cotangent, keys, values):
    members = keys.shape[0]
    width = GROUP_SHARE * HEAD_SIZE
    row_block = pl.BlockSpec((QUERY_LENGTH, width), lambda c, h, lens: (c, h))
    key_block = pl.BlockSpec((None, KEY_ROWS, HEAD_SIZE), lambda c, h, lens: (c, 0, h))
    grid_spec = pltpu.PrefetchScalarGridSpec(
        num_scalar_prefetch=1,
        grid=(members, KV_HEADS),
        in_specs=[row_block, row_block, key_block, key_block],
        out_specs=[row_block, key_block, key_block],
    )
    return pl.pallas_call(
        attention_kernel,
        grid_spec=grid_spec,
        out_shape=[
            jax.ShapeDtypeStruct(queries.shape, jnp.bfloat16),
            jax.ShapeDtypeStruct(keys.shape, jnp.float32),
            jax.ShapeDtypeStruct(keys.shape, jnp.float32),
        ],
    )(lens, queries, cotangent, keys, values)


def body(queries, suffix_key_value, output_gradient, node_kv, paths, tile_lens):
    members = paths.shape[0]
    span_width = node_kv.shape[-1]
    cores = lax.psum(1, "core")
    chips = lax.psum(1, "chip")
    node_count = cores * chips
    trie_node_rows = DEPTH * TILE_SLOTS
    portion = lax.all_gather(node_kv, "chip", axis=0, tiled=True)
    portion = lax.all_gather(portion, "core", axis=0, tiled=True)
    node_ids = jnp.clip(paths, 0, node_count - 1)
    where_held = (node_ids % cores) * chips + node_ids // cores
    path_tiles = jnp.take(portion, where_held.reshape(-1), axis=0).reshape(
        (members, DEPTH) + node_kv.shape[1:]
    )
    suffix_rows = suffix_key_value.reshape(2, members, QUERY_LENGTH, span_width)
    keys = jnp.concatenate(
        [path_tiles[:, :, 0].reshape(members, trie_node_rows, span_width), suffix_rows[0]], axis=1
    )
    values = jnp.concatenate(
        [path_tiles[:, :, 1].reshape(members, trie_node_rows, span_width), suffix_rows[1]], axis=1
    )
    lens = jnp.take(tile_lens, node_ids).astype(jnp.int32)
    query_out, key_gradient, value_gradient = attention(
        lens, queries, output_gradient, keys, values
    )
    suffix_out = jnp.stack(
        [key_gradient[:, trie_node_rows:], value_gradient[:, trie_node_rows:]], axis=0
    ).reshape(2, members * QUERY_LENGTH, span_width).astype(jnp.bfloat16)
    terms = jnp.stack(
        [
            key_gradient[:, :trie_node_rows].reshape(members, DEPTH, TILE_SLOTS, span_width),
            value_gradient[:, :trie_node_rows].reshape(members, DEPTH, TILE_SLOTS, span_width),
        ],
        axis=2,
    )
    block_sum = jnp.zeros((node_count,) + node_kv.shape[1:], jnp.bfloat16)
    merged = [terms[0]]
    for c in range(1, members):
        same = (node_ids[c] == node_ids[0])[:, None, None, None]
        merged[0] = merged[0] + jnp.where(same, terms[c], 0.0)
    merged[0] = merged[0].astype(jnp.bfloat16)
    for c in range(1, members):
        same = (node_ids[c] == node_ids[0])[:, None, None, None]
        merged.append(jnp.where(same, merged[0].astype(jnp.float32), terms[c]).astype(jnp.bfloat16))
    for c in range(members):
        for level in range(DEPTH):
            block_sum = lax.dynamic_update_slice(
                block_sum, merged[c][level][None], (where_held[c, level], 0, 0, 0)
            )
    partial = lax.psum_scatter(block_sum, "core", scatter_dimension=0, tiled=True)
    node_out = lax.psum_scatter(partial, "chip", scatter_dimension=0, tiled=True)
    return (query_out, suffix_out, node_out)


def solution(mesh):
    chips = mesh.shape["comp"] // 2
    devices = mesh.devices.reshape(chips, 2, mesh.shape["prompt"])
    split_mesh = Mesh(devices, ("chip", "core", "prompt"))
    rows = ("prompt", "chip", "core")
    in_specs = (
        P(rows, None),
        P(None, rows, None),
        P(rows, None),
        P(rows, None, None, None),
        P(rows, None),
        P("prompt"),
    )
    out_specs = (
        P(rows, None),
        P(None, rows, None),
        P(rows, None, None, None),
    )
    return jax.shard_map(
        body, mesh=split_mesh, in_specs=in_specs, out_specs=out_specs, check_vma=False
    )
```

```python
import math

import jax
import jax.numpy as jnp
from jax import lax
from jax.experimental import pallas as pl
from jax.experimental.pallas import tpu as pltpu
from jax.sharding import PartitionSpec as P

QUERY_HEADS = 20
KV_HEADS = 4
HEAD_SIZE = 128
TILE_SLOTS = 128
DEPTH = 4
QUERY_LENGTH = 128
GROUP_SHARE = QUERY_HEADS // KV_HEADS
NODE_ROWS = DEPTH * TILE_SLOTS
KEY_ROWS = NODE_ROWS + QUERY_LENGTH
STACK_ROWS = GROUP_SHARE * QUERY_LENGTH


def attention_kernel(ids_ref, lens_ref, q_ref, do_ref, *refs):
    node_k = refs[0:DEPTH]
    node_v = refs[DEPTH : 2 * DEPTH]
    own_k, own_v, dq_ref, dk_ref, dv_ref = refs[2 * DEPTH :]
    c = pl.program_id(1)
    factor = 1.0 / math.sqrt(HEAD_SIZE)
    key_block = jnp.concatenate([r[...] for r in node_k] + [own_k[...]], axis=0)
    value_block = jnp.concatenate([r[...] for r in node_v] + [own_v[...]], axis=0)
    heads = [slice(g * HEAD_SIZE, (g + 1) * HEAD_SIZE) for g in range(GROUP_SHARE)]
    query_rows = jnp.concatenate([q_ref[:, cols] for cols in heads], axis=0)
    cot_rows = jnp.concatenate([do_ref[:, cols] for cols in heads], axis=0)
    col = lax.broadcasted_iota(jnp.int32, (STACK_ROWS, KEY_ROWS), 1)
    row = lax.broadcasted_iota(jnp.int32, (STACK_ROWS, KEY_ROWS), 0) % QUERY_LENGTH
    level = col // TILE_SLOTS
    slot = col % TILE_SLOTS
    limit = jnp.where(
        level == 0,
        lens_ref[c, 0],
        jnp.where(level == 1, lens_ref[c, 1], jnp.where(level == 2, lens_ref[c, 2], lens_ref[c, 3])),
    )
    visible = ((level < DEPTH) & (slot < limit)) | ((level >= DEPTH) & ((col - NODE_ROWS) <= row))
    nt = (((1,), (1,)), ((), ()))
    tn = (((0,), (0,)), ((), ()))
    scores = lax.dot_general(query_rows, key_block, nt, preferred_element_type=jnp.float32) * factor
    scores = jnp.where(visible, scores, -jnp.inf)
    top = jnp.max(scores, axis=-1, keepdims=True)
    weights = jnp.exp(scores - top)
    probs = weights / jnp.sum(weights, axis=-1, keepdims=True)
    probs_low = probs.astype(jnp.bfloat16)
    outputs = jnp.dot(probs_low, value_block, preferred_element_type=jnp.float32)
    centre = jnp.sum(cot_rows.astype(jnp.float32) * outputs, axis=-1, keepdims=True)
    prob_grads = lax.dot_general(cot_rows, value_block, nt, preferred_element_type=jnp.float32)
    score_low = (probs * (prob_grads - centre)).astype(jnp.bfloat16)
    dq = (jnp.dot(score_low, key_block, preferred_element_type=jnp.float32) * factor).astype(jnp.bfloat16)
    for g, cols in enumerate(heads):
        dq_ref[:, cols] = dq[g * QUERY_LENGTH : (g + 1) * QUERY_LENGTH]
    dk = lax.dot_general(score_low, query_rows, tn, preferred_element_type=jnp.float32) * factor
    dv = lax.dot_general(probs_low, cot_rows, tn, preferred_element_type=jnp.float32)

    @pl.when(c == 0)
    def _():
        dk_ref[0] = dk
        dv_ref[0] = dv

    @pl.when(c == 1)
    def _():
        for level_at in range(DEPTH):
            rows = slice(level_at * TILE_SLOTS, (level_at + 1) * TILE_SLOTS)
            same = ids_ref[0, level_at] == ids_ref[1, level_at]
            for out_ref, term in ((dk_ref, dk), (dv_ref, dv)):
                before = out_ref[0, rows, :]
                here = term[rows]
                summed = before + here
                out_ref[0, rows, :] = jnp.where(same, summed, before)
                out_ref[1, rows, :] = jnp.where(same, summed, here)
        dk_ref[1, NODE_ROWS:, :] = dk[NODE_ROWS:]
        dv_ref[1, NODE_ROWS:, :] = dv[NODE_ROWS:]


def attention(ids, lens, queries, cotangent, portion, suffix_key_value):
    members = ids.shape[0]
    width = GROUP_SHARE * HEAD_SIZE
    row_block = pl.BlockSpec((QUERY_LENGTH, width), lambda h, c, ids, lens: (c, h))

    def node_block(level_at, half):
        return pl.BlockSpec(
            (None, None, TILE_SLOTS, HEAD_SIZE),
            lambda h, c, ids, lens: (ids[c, level_at], half, 0, h),
        )

    def own_block(half):
        return pl.BlockSpec((None, QUERY_LENGTH, HEAD_SIZE), lambda h, c, ids, lens: (half, c, h))

    grad_block = pl.BlockSpec((members, KEY_ROWS, HEAD_SIZE), lambda h, c, ids, lens: (0, 0, h))
    in_specs = (
        [row_block, row_block]
        + [node_block(level_at, 0) for level_at in range(DEPTH)]
        + [node_block(level_at, 1) for level_at in range(DEPTH)]
        + [own_block(0), own_block(1)]
    )
    grid_spec = pltpu.PrefetchScalarGridSpec(
        num_scalar_prefetch=2,
        grid=(KV_HEADS, members),
        in_specs=in_specs,
        out_specs=[row_block, grad_block, grad_block],
    )
    grad_shape = jax.ShapeDtypeStruct((members, KEY_ROWS, KV_HEADS * HEAD_SIZE), jnp.float32)
    return pl.pallas_call(
        attention_kernel,
        grid_spec=grid_spec,
        out_shape=[jax.ShapeDtypeStruct(queries.shape, jnp.bfloat16), grad_shape, grad_shape],
        compiler_params=pltpu.CompilerParams(vmem_limit_bytes=48 * 1024 * 1024),
    )(ids, lens, queries, cotangent, *([portion] * (2 * DEPTH)), suffix_key_value, suffix_key_value)


def body(queries, suffix_key_value, output_gradient, node_kv, paths, tile_lens):
    members = paths.shape[0]
    span_width = node_kv.shape[-1]
    portion = lax.all_gather(node_kv, "comp", axis=0, tiled=True)
    node_count = portion.shape[0]
    ids = jnp.clip(paths, 0, node_count - 1).astype(jnp.int32)
    lens = jnp.take(tile_lens, ids).astype(jnp.int32)
    query_out, key_gradient, value_gradient = attention(
        ids, lens, queries, output_gradient, portion, suffix_key_value
    )
    suffix_out = jnp.stack(
        [key_gradient[:, NODE_ROWS:], value_gradient[:, NODE_ROWS:]], axis=0
    ).reshape(2, members * QUERY_LENGTH, span_width).astype(jnp.bfloat16)
    slots = ids.reshape(members * DEPTH)
    hits = slots[None, :] == jnp.arange(node_count, dtype=jnp.int32)[:, None]
    slot_of = jnp.argmax(hits, axis=1)
    held = jnp.any(hits, axis=1)[:, None, None, None]
    slot_grads = jnp.stack(
        [
            key_gradient[:, :NODE_ROWS].reshape(members * DEPTH, TILE_SLOTS, span_width),
            value_gradient[:, :NODE_ROWS].reshape(members * DEPTH, TILE_SLOTS, span_width),
        ],
        axis=1,
    )
    block_sum = jnp.where(held, jnp.take(slot_grads, slot_of, axis=0), 0.0).astype(jnp.bfloat16)
    node_out = lax.psum_scatter(block_sum, "comp", scatter_dimension=0, tiled=True)
    return (query_out, suffix_out, node_out)


def solution(mesh):
    rows = ("prompt", "comp")
    in_specs = (
        P(rows, None),
        P(None, rows, None),
        P(rows, None),
        P(rows, None, None, None),
        P(rows, None),
        P("prompt"),
    )
    out_specs = (
        P(rows, None),
        P(None, rows, None),
        P(rows, None, None, None),
    )
    return jax.shard_map(body, mesh=mesh, in_specs=in_specs, out_specs=out_specs, check_vma=False)
```

```python
import math

import jax
import jax.numpy as jnp
from jax import lax
from jax.experimental import pallas as pl
from jax.experimental.pallas import tpu as pltpu
from jax.sharding import PartitionSpec as P

QUERY_HEADS = 20
KV_HEADS = 4
HEAD_SIZE = 128
TILE_SLOTS = 128
DEPTH = 4
QUERY_LENGTH = 128
GROUP_SHARE = QUERY_HEADS // KV_HEADS
NODE_ROWS = DEPTH * TILE_SLOTS
KEY_ROWS = NODE_ROWS + QUERY_LENGTH
STACK_ROWS = GROUP_SHARE * QUERY_LENGTH


def attention_kernel(ids_ref, lens_ref, q_ref, do_ref, *refs):
    node_k = refs[0:DEPTH]
    node_v = refs[DEPTH : 2 * DEPTH]
    own_k, own_v, dq_ref, own_out, sum_ref, keep_k, keep_v = refs[2 * DEPTH :]
    c = pl.program_id(1)
    factor = 1.0 / math.sqrt(HEAD_SIZE)
    key_block = jnp.concatenate([r[...] for r in node_k] + [own_k[...]], axis=0)
    value_block = jnp.concatenate([r[...] for r in node_v] + [own_v[...]], axis=0)
    heads = [slice(g * HEAD_SIZE, (g + 1) * HEAD_SIZE) for g in range(GROUP_SHARE)]
    query_rows = jnp.concatenate([q_ref[:, cols] for cols in heads], axis=0)
    cot_rows = jnp.concatenate([do_ref[:, cols] for cols in heads], axis=0)
    col = lax.broadcasted_iota(jnp.int32, (STACK_ROWS, KEY_ROWS), 1)
    row = lax.broadcasted_iota(jnp.int32, (STACK_ROWS, KEY_ROWS), 0) % QUERY_LENGTH
    level = col // TILE_SLOTS
    slot = col % TILE_SLOTS
    limit = jnp.where(
        level == 0,
        lens_ref[c, 0],
        jnp.where(level == 1, lens_ref[c, 1], jnp.where(level == 2, lens_ref[c, 2], lens_ref[c, 3])),
    )
    visible = ((level < DEPTH) & (slot < limit)) | ((level >= DEPTH) & ((col - NODE_ROWS) <= row))
    nt = (((1,), (1,)), ((), ()))
    tn = (((0,), (0,)), ((), ()))
    scores = lax.dot_general(query_rows, key_block, nt, preferred_element_type=jnp.float32) * factor
    scores = jnp.where(visible, scores, -jnp.inf)
    top = jnp.max(scores, axis=-1, keepdims=True)
    weights = jnp.exp(scores - top)
    probs = weights / jnp.sum(weights, axis=-1, keepdims=True)
    probs_low = probs.astype(jnp.bfloat16)
    outputs = jnp.dot(probs_low, value_block, preferred_element_type=jnp.float32)
    centre = jnp.sum(cot_rows.astype(jnp.float32) * outputs, axis=-1, keepdims=True)
    prob_grads = lax.dot_general(cot_rows, value_block, nt, preferred_element_type=jnp.float32)
    score_low = (probs * (prob_grads - centre)).astype(jnp.bfloat16)
    dq = (jnp.dot(score_low, key_block, preferred_element_type=jnp.float32) * factor).astype(jnp.bfloat16)
    for g, cols in enumerate(heads):
        dq_ref[:, cols] = dq[g * QUERY_LENGTH : (g + 1) * QUERY_LENGTH]
    dk = lax.dot_general(score_low, query_rows, tn, preferred_element_type=jnp.float32) * factor
    dv = lax.dot_general(probs_low, cot_rows, tn, preferred_element_type=jnp.float32)
    own_out[0] = dk[NODE_ROWS:].astype(jnp.bfloat16)
    own_out[1] = dv[NODE_ROWS:].astype(jnp.bfloat16)

    @pl.when(c == 0)
    def _():
        keep_k[...] = dk[:NODE_ROWS]
        keep_v[...] = dv[:NODE_ROWS]

    @pl.when(c == 1)
    def _():
        sum_ref[...] = jnp.zeros(sum_ref.shape, sum_ref.dtype)
        for level_at in range(DEPTH):
            rows = slice(level_at * TILE_SLOTS, (level_at + 1) * TILE_SLOTS)
            same = ids_ref[0, level_at] == ids_ref[1, level_at]
            for half, before, here in ((0, keep_k[rows, :], dk[rows]), (1, keep_v[rows, :], dv[rows])):
                summed = before + here
                sum_ref[ids_ref[0, level_at], half] = jnp.where(same, summed, before).astype(jnp.bfloat16)
                sum_ref[ids_ref[1, level_at], half] = jnp.where(same, summed, here).astype(jnp.bfloat16)


def attention(ids, lens, queries, cotangent, portion, suffix_key_value):
    members = ids.shape[0]
    node_count = portion.shape[0]
    width = GROUP_SHARE * HEAD_SIZE
    row_block = pl.BlockSpec((QUERY_LENGTH, width), lambda h, c, ids, lens: (c, h))

    def node_block(level_at, half):
        return pl.BlockSpec(
            (None, None, TILE_SLOTS, HEAD_SIZE),
            lambda h, c, ids, lens: (ids[c, level_at], half, 0, h),
        )

    def own_block(half):
        return pl.BlockSpec((None, QUERY_LENGTH, HEAD_SIZE), lambda h, c, ids, lens: (half, c, h))

    own_out_block = pl.BlockSpec((2, QUERY_LENGTH, HEAD_SIZE), lambda h, c, ids, lens: (0, c, h))
    sum_block = pl.BlockSpec(
        (node_count, 2, TILE_SLOTS, HEAD_SIZE), lambda h, c, ids, lens: (0, 0, 0, h)
    )
    in_specs = (
        [row_block, row_block]
        + [node_block(level_at, 0) for level_at in range(DEPTH)]
        + [node_block(level_at, 1) for level_at in range(DEPTH)]
        + [own_block(0), own_block(1)]
    )
    grid_spec = pltpu.PrefetchScalarGridSpec(
        num_scalar_prefetch=2,
        grid=(KV_HEADS, members),
        in_specs=in_specs,
        out_specs=[row_block, own_out_block, sum_block],
        scratch_shapes=[
            pltpu.VMEM((NODE_ROWS, HEAD_SIZE), jnp.float32),
            pltpu.VMEM((NODE_ROWS, HEAD_SIZE), jnp.float32),
        ],
    )
    return pl.pallas_call(
        attention_kernel,
        grid_spec=grid_spec,
        out_shape=[
            jax.ShapeDtypeStruct(queries.shape, jnp.bfloat16),
            jax.ShapeDtypeStruct(suffix_key_value.shape, jnp.bfloat16),
            jax.ShapeDtypeStruct(portion.shape, jnp.bfloat16),
        ],
        compiler_params=pltpu.CompilerParams(vmem_limit_bytes=48 * 1024 * 1024),
    )(ids, lens, queries, cotangent, *([portion] * (2 * DEPTH)), suffix_key_value, suffix_key_value)


def body(queries, suffix_key_value, output_gradient, node_kv, paths, tile_lens):
    portion = lax.all_gather(node_kv, "comp", axis=0, tiled=True)
    ids = jnp.clip(paths, 0, portion.shape[0] - 1).astype(jnp.int32)
    lens = jnp.take(tile_lens, ids).astype(jnp.int32)
    query_out, suffix_out, block_sum = attention(
        ids, lens, queries, output_gradient, portion, suffix_key_value
    )
    node_out = lax.psum_scatter(block_sum, "comp", scatter_dimension=0, tiled=True)
    return (query_out, suffix_out, node_out)


def solution(mesh):
    rows = ("prompt", "comp")
    in_specs = (
        P(rows, None),
        P(None, rows, None),
        P(rows, None),
        P(rows, None, None, None),
        P(rows, None),
        P("prompt"),
    )
    out_specs = (
        P(rows, None),
        P(None, rows, None),
        P(rows, None, None, None),
    )
    return jax.shard_map(body, mesh=mesh, in_specs=in_specs, out_specs=out_specs, check_vma=False)
```

```python
import math

import jax
import jax.numpy as jnp
from jax import lax
from jax.experimental import pallas as pl
from jax.experimental.pallas import tpu as pltpu
from jax.sharding import PartitionSpec as P

QUERY_HEADS = 20
KV_HEADS = 4
HEAD_SIZE = 128
TILE_SLOTS = 128
DEPTH = 4
QUERY_LENGTH = 128
GROUP_SHARE = QUERY_HEADS // KV_HEADS
NODE_ROWS = DEPTH * TILE_SLOTS
KEY_ROWS = NODE_ROWS + QUERY_LENGTH
STACK_ROWS = GROUP_SHARE * QUERY_LENGTH


def attention_kernel(ids_ref, lens_ref, q_ref, do_ref, *refs):
    node_k = refs[0:DEPTH]
    node_v = refs[DEPTH : 2 * DEPTH]
    own_k, own_v, dq_ref, own_out, sum_ref, keep_k, keep_v = refs[2 * DEPTH :]
    c = pl.program_id(1)
    factor = 1.0 / math.sqrt(HEAD_SIZE)
    key_block = jnp.concatenate([r[...] for r in node_k] + [own_k[...]], axis=0)
    value_block = jnp.concatenate([r[...] for r in node_v] + [own_v[...]], axis=0)
    heads = [slice(g * HEAD_SIZE, (g + 1) * HEAD_SIZE) for g in range(GROUP_SHARE)]
    query_rows = jnp.concatenate([q_ref[:, cols] for cols in heads], axis=0)
    cot_rows = jnp.concatenate([do_ref[:, cols] for cols in heads], axis=0)
    col = lax.broadcasted_iota(jnp.int32, (STACK_ROWS, KEY_ROWS), 1)
    row = lax.broadcasted_iota(jnp.int32, (STACK_ROWS, KEY_ROWS), 0) % QUERY_LENGTH
    level = col // TILE_SLOTS
    slot = col % TILE_SLOTS
    limit = jnp.where(
        level == 0,
        lens_ref[c, 0],
        jnp.where(level == 1, lens_ref[c, 1], jnp.where(level == 2, lens_ref[c, 2], lens_ref[c, 3])),
    )
    visible = ((level < DEPTH) & (slot < limit)) | ((level >= DEPTH) & ((col - NODE_ROWS) <= row))
    nt = (((1,), (1,)), ((), ()))
    tn = (((0,), (0,)), ((), ()))
    scores = lax.dot_general(query_rows, key_block, nt, preferred_element_type=jnp.float32) * factor
    scores = jnp.where(visible, scores, -jnp.inf)
    top = jnp.max(scores, axis=-1, keepdims=True)
    weights = jnp.exp(scores - top)
    probs = weights / jnp.sum(weights, axis=-1, keepdims=True)
    probs_low = probs.astype(jnp.bfloat16)
    outputs = jnp.dot(probs_low, value_block, preferred_element_type=jnp.float32)
    centre = jnp.sum(cot_rows.astype(jnp.float32) * outputs, axis=-1, keepdims=True)
    prob_grads = lax.dot_general(cot_rows, value_block, nt, preferred_element_type=jnp.float32)
    score_low = (probs * (prob_grads - centre)).astype(jnp.bfloat16)
    dq = (jnp.dot(score_low, key_block, preferred_element_type=jnp.float32) * factor).astype(jnp.bfloat16)
    for g, cols in enumerate(heads):
        dq_ref[:, cols] = dq[g * QUERY_LENGTH : (g + 1) * QUERY_LENGTH]
    dk = lax.dot_general(score_low, query_rows, tn, preferred_element_type=jnp.float32) * factor
    dv = lax.dot_general(probs_low, cot_rows, tn, preferred_element_type=jnp.float32)
    own_out[0] = dk[NODE_ROWS:].astype(jnp.bfloat16)
    own_out[1] = dv[NODE_ROWS:].astype(jnp.bfloat16)

    @pl.when(c == 0)
    def _():
        keep_k[...] = dk[:NODE_ROWS]
        keep_v[...] = dv[:NODE_ROWS]

    @pl.when(c == 1)
    def _():
        sum_ref[...] = jnp.zeros(sum_ref.shape, sum_ref.dtype)
        for level_at in range(DEPTH):
            rows = slice(level_at * TILE_SLOTS, (level_at + 1) * TILE_SLOTS)
            same = ids_ref[0, level_at] == ids_ref[1, level_at]
            for half, before, here in ((0, keep_k[rows, :], dk[rows]), (1, keep_v[rows, :], dv[rows])):
                summed = before + here
                sum_ref[ids_ref[0, level_at], half] = jnp.where(same, summed, before).astype(jnp.bfloat16)
                sum_ref[ids_ref[1, level_at], half] = jnp.where(same, summed, here).astype(jnp.bfloat16)


def attention(ids, lens, queries, cotangent, portion, suffix_key_value):
    members = ids.shape[0]
    node_count = portion.shape[0]
    width = GROUP_SHARE * HEAD_SIZE
    row_block = pl.BlockSpec((QUERY_LENGTH, width), lambda h, c, ids, lens: (c, h))

    def node_block(level_at, half):
        return pl.BlockSpec(
            (None, None, TILE_SLOTS, HEAD_SIZE),
            lambda h, c, ids, lens: (ids[c, level_at], half, 0, h),
        )

    def own_block(half):
        return pl.BlockSpec((None, QUERY_LENGTH, HEAD_SIZE), lambda h, c, ids, lens: (half, c, h))

    own_out_block = pl.BlockSpec((2, QUERY_LENGTH, HEAD_SIZE), lambda h, c, ids, lens: (0, c, h))
    sum_block = pl.BlockSpec(
        (node_count, 2, TILE_SLOTS, HEAD_SIZE), lambda h, c, ids, lens: (0, 0, 0, h)
    )
    in_specs = (
        [row_block, row_block]
        + [node_block(level_at, 0) for level_at in range(DEPTH)]
        + [node_block(level_at, 1) for level_at in range(DEPTH)]
        + [own_block(0), own_block(1)]
    )
    grid_spec = pltpu.PrefetchScalarGridSpec(
        num_scalar_prefetch=2,
        grid=(KV_HEADS, members),
        in_specs=in_specs,
        out_specs=[row_block, own_out_block, sum_block],
        scratch_shapes=[
            pltpu.VMEM((NODE_ROWS, HEAD_SIZE), jnp.float32),
            pltpu.VMEM((NODE_ROWS, HEAD_SIZE), jnp.float32),
        ],
    )
    return pl.pallas_call(
        attention_kernel,
        grid_spec=grid_spec,
        out_shape=[
            jax.ShapeDtypeStruct(queries.shape, jnp.bfloat16),
            jax.ShapeDtypeStruct(suffix_key_value.shape, jnp.bfloat16),
            jax.ShapeDtypeStruct(portion.shape, jnp.bfloat16),
        ],
        compiler_params=pltpu.CompilerParams(vmem_limit_bytes=48 * 1024 * 1024),
    )(ids, lens, queries, cotangent, *([portion] * (2 * DEPTH)), suffix_key_value, suffix_key_value)


def body(queries, suffix_key_value, output_gradient, node_kv, paths, tile_lens):
    portion = lax.all_gather(node_kv, "comp", axis=0, tiled=True)
    ids = jnp.clip(paths, 0, portion.shape[0] - 1).astype(jnp.int32)
    lens = jnp.take(tile_lens, ids).astype(jnp.int32)
    query_out, suffix_out, block_sum = attention(
        ids, lens, queries, output_gradient, portion, suffix_key_value
    )
    received = lax.all_to_all(block_sum, "comp", 0, 0, tiled=True)
    node_out = jnp.sum(received.astype(jnp.float32), axis=0, keepdims=True).astype(jnp.bfloat16)
    return (query_out, suffix_out, node_out)


def solution(mesh):
    rows = ("prompt", "comp")
    in_specs = (
        P(rows, None),
        P(None, rows, None),
        P(rows, None),
        P(rows, None, None, None),
        P(rows, None),
        P("prompt"),
    )
    out_specs = (
        P(rows, None),
        P(None, rows, None),
        P(rows, None, None, None),
    )
    return jax.shard_map(body, mesh=mesh, in_specs=in_specs, out_specs=out_specs, check_vma=False)
```

```python
import math

import jax
import jax.numpy as jnp
from jax import lax
from jax.experimental import pallas as pl
from jax.experimental.pallas import tpu as pltpu
from jax.sharding import PartitionSpec as P

QUERY_HEADS = 20
KV_HEADS = 4
HEAD_SIZE = 128
TILE_SLOTS = 128
DEPTH = 4
QUERY_LENGTH = 128
GROUP_SHARE = QUERY_HEADS // KV_HEADS
NODE_ROWS = DEPTH * TILE_SLOTS
KEY_ROWS = NODE_ROWS + QUERY_LENGTH
STACK_ROWS = GROUP_SHARE * QUERY_LENGTH


def attention_kernel(ids_ref, lens_ref, bias_ref, q_ref, do_ref, *refs):
    node_k = refs[0:DEPTH]
    node_v = refs[DEPTH : 2 * DEPTH]
    own_k, own_v, dq_ref, own_out, sum_ref, keep_k, keep_v = refs[2 * DEPTH :]
    c = pl.program_id(1)
    factor = 1.0 / math.sqrt(HEAD_SIZE)
    key_block = jnp.concatenate([r[...] for r in node_k] + [own_k[...]], axis=0)
    value_block = jnp.concatenate([r[...] for r in node_v] + [own_v[...]], axis=0)
    heads = [slice(g * HEAD_SIZE, (g + 1) * HEAD_SIZE) for g in range(GROUP_SHARE)]
    query_rows = jnp.concatenate([q_ref[:, cols] for cols in heads], axis=0)
    cot_rows = jnp.concatenate([do_ref[:, cols] for cols in heads], axis=0)
    nt = (((1,), (1,)), ((), ()))
    tn = (((0,), (0,)), ((), ()))
    scores = lax.dot_general(query_rows, key_block, nt, preferred_element_type=jnp.float32) * factor
    scores = (scores.reshape(GROUP_SHARE, QUERY_LENGTH, KEY_ROWS) + bias_ref[...][None]).reshape(
        STACK_ROWS, KEY_ROWS
    )
    top = jnp.max(scores, axis=-1, keepdims=True)
    weights = jnp.exp(scores - top)
    probs = weights * (1.0 / jnp.sum(weights, axis=-1, keepdims=True))
    probs_low = probs.astype(jnp.bfloat16)
    outputs = jnp.dot(probs_low, value_block, preferred_element_type=jnp.float32)
    centre = jnp.sum(cot_rows.astype(jnp.float32) * outputs, axis=-1, keepdims=True)
    prob_grads = lax.dot_general(cot_rows, value_block, nt, preferred_element_type=jnp.float32)
    score_low = (probs * (prob_grads - centre)).astype(jnp.bfloat16)
    dq = (jnp.dot(score_low, key_block, preferred_element_type=jnp.float32) * factor).astype(jnp.bfloat16)
    for g, cols in enumerate(heads):
        dq_ref[:, cols] = dq[g * QUERY_LENGTH : (g + 1) * QUERY_LENGTH]
    dk = lax.dot_general(score_low, query_rows, tn, preferred_element_type=jnp.float32) * factor
    dv = lax.dot_general(probs_low, cot_rows, tn, preferred_element_type=jnp.float32)
    own_out[0] = dk[NODE_ROWS:].astype(jnp.bfloat16)
    own_out[1] = dv[NODE_ROWS:].astype(jnp.bfloat16)

    @pl.when(c == 0)
    def _():
        keep_k[...] = dk[:NODE_ROWS]
        keep_v[...] = dv[:NODE_ROWS]

    @pl.when(c == 1)
    def _():
        sum_ref[...] = jnp.zeros(sum_ref.shape, sum_ref.dtype)
        for level_at in range(DEPTH):
            rows = slice(level_at * TILE_SLOTS, (level_at + 1) * TILE_SLOTS)
            same = ids_ref[0, level_at] == ids_ref[1, level_at]
            for half, before, here in ((0, keep_k[rows, :], dk[rows]), (1, keep_v[rows, :], dv[rows])):
                summed = before + here
                sum_ref[ids_ref[0, level_at], half] = jnp.where(same, summed, before).astype(jnp.bfloat16)
                sum_ref[ids_ref[1, level_at], half] = jnp.where(same, summed, here).astype(jnp.bfloat16)


def attention(ids, lens, bias, queries, cotangent, portion, suffix_key_value):
    members = ids.shape[0]
    node_count = portion.shape[0]
    width = GROUP_SHARE * HEAD_SIZE
    row_block = pl.BlockSpec((QUERY_LENGTH, width), lambda h, c, ids, lens: (c, h))

    def node_block(level_at, half):
        return pl.BlockSpec(
            (None, None, TILE_SLOTS, HEAD_SIZE),
            lambda h, c, ids, lens: (ids[c, level_at], half, 0, h),
        )

    def own_block(half):
        return pl.BlockSpec((None, QUERY_LENGTH, HEAD_SIZE), lambda h, c, ids, lens: (half, c, h))

    own_out_block = pl.BlockSpec((2, QUERY_LENGTH, HEAD_SIZE), lambda h, c, ids, lens: (0, c, h))
    sum_block = pl.BlockSpec(
        (node_count, 2, TILE_SLOTS, HEAD_SIZE), lambda h, c, ids, lens: (0, 0, 0, h)
    )
    bias_block = pl.BlockSpec((None, QUERY_LENGTH, KEY_ROWS), lambda h, c, ids, lens: (c, 0, 0))
    in_specs = (
        [bias_block, row_block, row_block]
        + [node_block(level_at, 0) for level_at in range(DEPTH)]
        + [node_block(level_at, 1) for level_at in range(DEPTH)]
        + [own_block(0), own_block(1)]
    )
    grid_spec = pltpu.PrefetchScalarGridSpec(
        num_scalar_prefetch=2,
        grid=(KV_HEADS, members),
        in_specs=in_specs,
        out_specs=[row_block, own_out_block, sum_block],
        scratch_shapes=[
            pltpu.VMEM((NODE_ROWS, HEAD_SIZE), jnp.float32),
            pltpu.VMEM((NODE_ROWS, HEAD_SIZE), jnp.float32),
        ],
    )
    return pl.pallas_call(
        attention_kernel,
        grid_spec=grid_spec,
        out_shape=[
            jax.ShapeDtypeStruct(queries.shape, jnp.bfloat16),
            jax.ShapeDtypeStruct(suffix_key_value.shape, jnp.bfloat16),
            jax.ShapeDtypeStruct(portion.shape, jnp.bfloat16),
        ],
        compiler_params=pltpu.CompilerParams(vmem_limit_bytes=48 * 1024 * 1024),
    )(ids, lens, bias, queries, cotangent, *([portion] * (2 * DEPTH)), suffix_key_value, suffix_key_value)


def body(queries, suffix_key_value, output_gradient, node_kv, paths, tile_lens):
    portion = lax.all_gather(node_kv, "comp", axis=0, tiled=True)
    ids = jnp.clip(paths, 0, portion.shape[0] - 1).astype(jnp.int32)
    lens = jnp.take(tile_lens, ids).astype(jnp.int32)
    slot = jnp.arange(TILE_SLOTS, dtype=jnp.int32)
    node_seen = (slot[None, None, :] < lens[:, :, None]).reshape(lens.shape[0], 1, NODE_ROWS)
    own = jnp.arange(QUERY_LENGTH, dtype=jnp.int32)
    causal = (own[None, :] <= own[:, None])[None]
    visible = jnp.concatenate(
        [
            jnp.broadcast_to(node_seen, (lens.shape[0], QUERY_LENGTH, NODE_ROWS)),
            jnp.broadcast_to(causal, (lens.shape[0], QUERY_LENGTH, QUERY_LENGTH)),
        ],
        axis=2,
    )
    bias = jnp.where(visible, 0.0, -jnp.inf).astype(jnp.float32)
    query_out, suffix_out, block_sum = attention(
        ids, lens, bias, queries, output_gradient, portion, suffix_key_value
    )
    node_out = lax.psum_scatter(block_sum, "comp", scatter_dimension=0, tiled=True)
    return (query_out, suffix_out, node_out)


def solution(mesh):
    rows = ("prompt", "comp")
    in_specs = (
        P(rows, None),
        P(None, rows, None),
        P(rows, None),
        P(rows, None, None, None),
        P(rows, None),
        P("prompt"),
    )
    out_specs = (
        P(rows, None),
        P(None, rows, None),
        P(rows, None, None, None),
    )
    return jax.shard_map(body, mesh=mesh, in_specs=in_specs, out_specs=out_specs, check_vma=False)
```

```python
import math

import jax
import jax.numpy as jnp
from jax import lax
from jax.experimental import pallas as pl
from jax.experimental.pallas import tpu as pltpu
from jax.sharding import PartitionSpec as P

QUERY_HEADS = 20
KV_HEADS = 4
HEAD_SIZE = 128
TILE_SLOTS = 128
DEPTH = 4
QUERY_LENGTH = 128
GROUP_SHARE = QUERY_HEADS // KV_HEADS
NODE_ROWS = DEPTH * TILE_SLOTS
KEY_ROWS = NODE_ROWS + QUERY_LENGTH
STACK_ROWS = GROUP_SHARE * QUERY_LENGTH


HEADS_AT_ONCE = 2


def attention_kernel(ids_ref, lens_ref, bias_ref, q_ref, do_ref, *refs):
    node_k = refs[0:DEPTH]
    node_v = refs[DEPTH : 2 * DEPTH]
    own_k, own_v, dq_ref, own_out, sum_ref, keep_k, keep_v = refs[2 * DEPTH :]
    c = pl.program_id(1)
    factor = 1.0 / math.sqrt(HEAD_SIZE)
    nt = (((1,), (1,)), ((), ()))
    tn = (((0,), (0,)), ((), ()))
    bias = bias_ref[...][None]
    width = GROUP_SHARE * HEAD_SIZE
    grads = []
    for sub in range(HEADS_AT_ONCE):
        lanes = slice(sub * HEAD_SIZE, (sub + 1) * HEAD_SIZE)
        key_block = jnp.concatenate([r[:, lanes] for r in node_k] + [own_k[:, lanes]], axis=0)
        value_block = jnp.concatenate([r[:, lanes] for r in node_v] + [own_v[:, lanes]], axis=0)
        heads = [
            slice(sub * width + g * HEAD_SIZE, sub * width + (g + 1) * HEAD_SIZE)
            for g in range(GROUP_SHARE)
        ]
        query_rows = jnp.concatenate([q_ref[:, cols] for cols in heads], axis=0)
        cot_rows = jnp.concatenate([do_ref[:, cols] for cols in heads], axis=0)
        scores = lax.dot_general(query_rows, key_block, nt, preferred_element_type=jnp.float32) * factor
        scores = (scores.reshape(GROUP_SHARE, QUERY_LENGTH, KEY_ROWS) + bias).reshape(
            STACK_ROWS, KEY_ROWS
        )
        top = jnp.max(scores, axis=-1, keepdims=True)
        weights = jnp.exp(scores - top)
        probs = weights * (1.0 / jnp.sum(weights, axis=-1, keepdims=True))
        probs_low = probs.astype(jnp.bfloat16)
        outputs = jnp.dot(probs_low, value_block, preferred_element_type=jnp.float32)
        centre = jnp.sum(cot_rows.astype(jnp.float32) * outputs, axis=-1, keepdims=True)
        prob_grads = lax.dot_general(cot_rows, value_block, nt, preferred_element_type=jnp.float32)
        score_low = (probs * (prob_grads - centre)).astype(jnp.bfloat16)
        dq = (jnp.dot(score_low, key_block, preferred_element_type=jnp.float32) * factor).astype(
            jnp.bfloat16
        )
        for g, cols in enumerate(heads):
            dq_ref[:, cols] = dq[g * QUERY_LENGTH : (g + 1) * QUERY_LENGTH]
        dk = lax.dot_general(score_low, query_rows, tn, preferred_element_type=jnp.float32) * factor
        dv = lax.dot_general(probs_low, cot_rows, tn, preferred_element_type=jnp.float32)
        own_out[0, :, lanes] = dk[NODE_ROWS:].astype(jnp.bfloat16)
        own_out[1, :, lanes] = dv[NODE_ROWS:].astype(jnp.bfloat16)
        grads.append((lanes, dk, dv))

    @pl.when(c == 0)
    def _():
        for lanes, dk, dv in grads:
            keep_k[:, lanes] = dk[:NODE_ROWS]
            keep_v[:, lanes] = dv[:NODE_ROWS]

    @pl.when(c == 1)
    def _():
        sum_ref[...] = jnp.zeros(sum_ref.shape, sum_ref.dtype)
        for level_at in range(DEPTH):
            rows = slice(level_at * TILE_SLOTS, (level_at + 1) * TILE_SLOTS)
            same = ids_ref[0, level_at] == ids_ref[1, level_at]
            for lanes, dk, dv in grads:
                for half, before, here in (
                    (0, keep_k[rows, lanes], dk[rows]),
                    (1, keep_v[rows, lanes], dv[rows]),
                ):
                    summed = before + here
                    sum_ref[ids_ref[0, level_at], half, :, lanes] = jnp.where(
                        same, summed, before
                    ).astype(jnp.bfloat16)
                    sum_ref[ids_ref[1, level_at], half, :, lanes] = jnp.where(
                        same, summed, here
                    ).astype(jnp.bfloat16)


def attention(ids, lens, bias, queries, cotangent, portion, suffix_key_value):
    members = ids.shape[0]
    node_count = portion.shape[0]
    width = HEADS_AT_ONCE * GROUP_SHARE * HEAD_SIZE
    lanes = HEADS_AT_ONCE * HEAD_SIZE
    row_block = pl.BlockSpec((QUERY_LENGTH, width), lambda h, c, ids, lens: (c, h))

    def node_block(level_at, half):
        return pl.BlockSpec(
            (None, None, TILE_SLOTS, lanes),
            lambda h, c, ids, lens: (ids[c, level_at], half, 0, h),
        )

    def own_block(half):
        return pl.BlockSpec((None, QUERY_LENGTH, lanes), lambda h, c, ids, lens: (half, c, h))

    own_out_block = pl.BlockSpec((2, QUERY_LENGTH, lanes), lambda h, c, ids, lens: (0, c, h))
    sum_block = pl.BlockSpec((node_count, 2, TILE_SLOTS, lanes), lambda h, c, ids, lens: (0, 0, 0, h))
    bias_block = pl.BlockSpec((None, QUERY_LENGTH, KEY_ROWS), lambda h, c, ids, lens: (c, 0, 0))
    in_specs = (
        [bias_block, row_block, row_block]
        + [node_block(level_at, 0) for level_at in range(DEPTH)]
        + [node_block(level_at, 1) for level_at in range(DEPTH)]
        + [own_block(0), own_block(1)]
    )
    grid_spec = pltpu.PrefetchScalarGridSpec(
        num_scalar_prefetch=2,
        grid=(KV_HEADS // HEADS_AT_ONCE, members),
        in_specs=in_specs,
        out_specs=[row_block, own_out_block, sum_block],
        scratch_shapes=[
            pltpu.VMEM((NODE_ROWS, lanes), jnp.float32),
            pltpu.VMEM((NODE_ROWS, lanes), jnp.float32),
        ],
    )
    return pl.pallas_call(
        attention_kernel,
        grid_spec=grid_spec,
        out_shape=[
            jax.ShapeDtypeStruct(queries.shape, jnp.bfloat16),
            jax.ShapeDtypeStruct(suffix_key_value.shape, jnp.bfloat16),
            jax.ShapeDtypeStruct(portion.shape, jnp.bfloat16),
        ],
        compiler_params=pltpu.CompilerParams(vmem_limit_bytes=56 * 1024 * 1024),
    )(ids, lens, bias, queries, cotangent, *([portion] * (2 * DEPTH)), suffix_key_value, suffix_key_value)


def body(queries, suffix_key_value, output_gradient, node_kv, paths, tile_lens):
    portion = lax.all_gather(node_kv, "comp", axis=0, tiled=True)
    ids = jnp.clip(paths, 0, portion.shape[0] - 1).astype(jnp.int32)
    lens = jnp.take(tile_lens, ids).astype(jnp.int32)
    slot = jnp.arange(TILE_SLOTS, dtype=jnp.int32)
    node_seen = (slot[None, None, :] < lens[:, :, None]).reshape(lens.shape[0], 1, NODE_ROWS)
    own = jnp.arange(QUERY_LENGTH, dtype=jnp.int32)
    causal = (own[None, :] <= own[:, None])[None]
    visible = jnp.concatenate(
        [
            jnp.broadcast_to(node_seen, (lens.shape[0], QUERY_LENGTH, NODE_ROWS)),
            jnp.broadcast_to(causal, (lens.shape[0], QUERY_LENGTH, QUERY_LENGTH)),
        ],
        axis=2,
    )
    bias = jnp.where(visible, 0.0, -jnp.inf).astype(jnp.float32)
    query_out, suffix_out, block_sum = attention(
        ids, lens, bias, queries, output_gradient, portion, suffix_key_value
    )
    node_out = lax.psum_scatter(block_sum, "comp", scatter_dimension=0, tiled=True)
    return (query_out, suffix_out, node_out)


def solution(mesh):
    rows = ("prompt", "comp")
    in_specs = (
        P(rows, None),
        P(None, rows, None),
        P(rows, None),
        P(rows, None, None, None),
        P(rows, None),
        P("prompt"),
    )
    out_specs = (
        P(rows, None),
        P(None, rows, None),
        P(rows, None, None, None),
    )
    return jax.shard_map(body, mesh=mesh, in_specs=in_specs, out_specs=out_specs, check_vma=False)
```

```python
import math

import jax
import jax.numpy as jnp
from jax import lax
from jax.experimental import pallas as pl
from jax.experimental.pallas import tpu as pltpu
from jax.sharding import PartitionSpec as P

QUERY_HEADS = 20
KV_HEADS = 4
HEAD_SIZE = 128
TILE_SLOTS = 128
DEPTH = 4
QUERY_LENGTH = 128
GROUP_SHARE = QUERY_HEADS // KV_HEADS
NODE_ROWS = DEPTH * TILE_SLOTS
KEY_ROWS = NODE_ROWS + QUERY_LENGTH
STACK_ROWS = GROUP_SHARE * QUERY_LENGTH


HEADS_AT_ONCE = 4


def attention_kernel(ids_ref, lens_ref, bias_ref, q_ref, do_ref, *refs):
    node_k = refs[0:DEPTH]
    node_v = refs[DEPTH : 2 * DEPTH]
    own_k, own_v, dq_ref, own_out, sum_ref, keep_k, keep_v = refs[2 * DEPTH :]
    c = pl.program_id(1)
    factor = 1.0 / math.sqrt(HEAD_SIZE)
    nt = (((1,), (1,)), ((), ()))
    tn = (((0,), (0,)), ((), ()))
    bias = bias_ref[...][None]
    width = GROUP_SHARE * HEAD_SIZE
    grads = []
    for sub in range(HEADS_AT_ONCE):
        lanes = slice(sub * HEAD_SIZE, (sub + 1) * HEAD_SIZE)
        key_block = jnp.concatenate([r[:, lanes] for r in node_k] + [own_k[:, lanes]], axis=0)
        value_block = jnp.concatenate([r[:, lanes] for r in node_v] + [own_v[:, lanes]], axis=0)
        heads = [
            slice(sub * width + g * HEAD_SIZE, sub * width + (g + 1) * HEAD_SIZE)
            for g in range(GROUP_SHARE)
        ]
        query_rows = jnp.concatenate([q_ref[:, cols] for cols in heads], axis=0)
        cot_rows = jnp.concatenate([do_ref[:, cols] for cols in heads], axis=0)
        scores = lax.dot_general(query_rows, key_block, nt, preferred_element_type=jnp.float32) * factor
        scores = (scores.reshape(GROUP_SHARE, QUERY_LENGTH, KEY_ROWS) + bias).reshape(
            STACK_ROWS, KEY_ROWS
        )
        top = jnp.max(scores, axis=-1, keepdims=True)
        weights = jnp.exp(scores - top)
        probs = weights * (1.0 / jnp.sum(weights, axis=-1, keepdims=True))
        probs_low = probs.astype(jnp.bfloat16)
        outputs = jnp.dot(probs_low, value_block, preferred_element_type=jnp.float32)
        centre = jnp.sum(cot_rows.astype(jnp.float32) * outputs, axis=-1, keepdims=True)
        prob_grads = lax.dot_general(cot_rows, value_block, nt, preferred_element_type=jnp.float32)
        score_low = (probs * (prob_grads - centre)).astype(jnp.bfloat16)
        dq = (jnp.dot(score_low, key_block, preferred_element_type=jnp.float32) * factor).astype(
            jnp.bfloat16
        )
        for g, cols in enumerate(heads):
            dq_ref[:, cols] = dq[g * QUERY_LENGTH : (g + 1) * QUERY_LENGTH]
        dk = lax.dot_general(score_low, query_rows, tn, preferred_element_type=jnp.float32) * factor
        dv = lax.dot_general(probs_low, cot_rows, tn, preferred_element_type=jnp.float32)
        own_out[0, :, lanes] = dk[NODE_ROWS:].astype(jnp.bfloat16)
        own_out[1, :, lanes] = dv[NODE_ROWS:].astype(jnp.bfloat16)
        grads.append((lanes, dk, dv))

    @pl.when(c == 0)
    def _():
        for lanes, dk, dv in grads:
            keep_k[:, lanes] = dk[:NODE_ROWS]
            keep_v[:, lanes] = dv[:NODE_ROWS]

    @pl.when(c == 1)
    def _():
        sum_ref[...] = jnp.zeros(sum_ref.shape, sum_ref.dtype)
        for level_at in range(DEPTH):
            rows = slice(level_at * TILE_SLOTS, (level_at + 1) * TILE_SLOTS)
            same = ids_ref[0, level_at] == ids_ref[1, level_at]
            for lanes, dk, dv in grads:
                for half, before, here in (
                    (0, keep_k[rows, lanes], dk[rows]),
                    (1, keep_v[rows, lanes], dv[rows]),
                ):
                    summed = before + here
                    sum_ref[ids_ref[0, level_at], half, :, lanes] = jnp.where(
                        same, summed, before
                    ).astype(jnp.bfloat16)
                    sum_ref[ids_ref[1, level_at], half, :, lanes] = jnp.where(
                        same, summed, here
                    ).astype(jnp.bfloat16)


def attention(ids, lens, bias, queries, cotangent, portion, suffix_key_value):
    members = ids.shape[0]
    node_count = portion.shape[0]
    width = HEADS_AT_ONCE * GROUP_SHARE * HEAD_SIZE
    lanes = HEADS_AT_ONCE * HEAD_SIZE
    row_block = pl.BlockSpec((QUERY_LENGTH, width), lambda h, c, ids, lens: (c, h))

    def node_block(level_at, half):
        return pl.BlockSpec(
            (None, None, TILE_SLOTS, lanes),
            lambda h, c, ids, lens: (ids[c, level_at], half, 0, h),
        )

    def own_block(half):
        return pl.BlockSpec((None, QUERY_LENGTH, lanes), lambda h, c, ids, lens: (half, c, h))

    own_out_block = pl.BlockSpec((2, QUERY_LENGTH, lanes), lambda h, c, ids, lens: (0, c, h))
    sum_block = pl.BlockSpec((node_count, 2, TILE_SLOTS, lanes), lambda h, c, ids, lens: (0, 0, 0, h))
    bias_block = pl.BlockSpec((None, QUERY_LENGTH, KEY_ROWS), lambda h, c, ids, lens: (c, 0, 0))
    in_specs = (
        [bias_block, row_block, row_block]
        + [node_block(level_at, 0) for level_at in range(DEPTH)]
        + [node_block(level_at, 1) for level_at in range(DEPTH)]
        + [own_block(0), own_block(1)]
    )
    grid_spec = pltpu.PrefetchScalarGridSpec(
        num_scalar_prefetch=2,
        grid=(KV_HEADS // HEADS_AT_ONCE, members),
        in_specs=in_specs,
        out_specs=[row_block, own_out_block, sum_block],
        scratch_shapes=[
            pltpu.VMEM((NODE_ROWS, lanes), jnp.float32),
            pltpu.VMEM((NODE_ROWS, lanes), jnp.float32),
        ],
    )
    return pl.pallas_call(
        attention_kernel,
        grid_spec=grid_spec,
        out_shape=[
            jax.ShapeDtypeStruct(queries.shape, jnp.bfloat16),
            jax.ShapeDtypeStruct(suffix_key_value.shape, jnp.bfloat16),
            jax.ShapeDtypeStruct(portion.shape, jnp.bfloat16),
        ],
        compiler_params=pltpu.CompilerParams(vmem_limit_bytes=56 * 1024 * 1024),
    )(ids, lens, bias, queries, cotangent, *([portion] * (2 * DEPTH)), suffix_key_value, suffix_key_value)


def body(queries, suffix_key_value, output_gradient, node_kv, paths, tile_lens):
    portion = lax.all_gather(node_kv, "comp", axis=0, tiled=True)
    ids = jnp.clip(paths, 0, portion.shape[0] - 1).astype(jnp.int32)
    lens = jnp.take(tile_lens, ids).astype(jnp.int32)
    slot = jnp.arange(TILE_SLOTS, dtype=jnp.int32)
    node_seen = (slot[None, None, :] < lens[:, :, None]).reshape(lens.shape[0], 1, NODE_ROWS)
    own = jnp.arange(QUERY_LENGTH, dtype=jnp.int32)
    causal = (own[None, :] <= own[:, None])[None]
    visible = jnp.concatenate(
        [
            jnp.broadcast_to(node_seen, (lens.shape[0], QUERY_LENGTH, NODE_ROWS)),
            jnp.broadcast_to(causal, (lens.shape[0], QUERY_LENGTH, QUERY_LENGTH)),
        ],
        axis=2,
    )
    bias = jnp.where(visible, 0.0, -jnp.inf).astype(jnp.float32)
    query_out, suffix_out, block_sum = attention(
        ids, lens, bias, queries, output_gradient, portion, suffix_key_value
    )
    node_out = lax.psum_scatter(block_sum, "comp", scatter_dimension=0, tiled=True)
    return (query_out, suffix_out, node_out)


def solution(mesh):
    rows = ("prompt", "comp")
    in_specs = (
        P(rows, None),
        P(None, rows, None),
        P(rows, None),
        P(rows, None, None, None),
        P(rows, None),
        P("prompt"),
    )
    out_specs = (
        P(rows, None),
        P(None, rows, None),
        P(rows, None, None, None),
    )
    return jax.shard_map(body, mesh=mesh, in_specs=in_specs, out_specs=out_specs, check_vma=False)
```
